768 devices in a mesh: face: 96 (over z_lo, y, core), tile: 8 (over x, z_hi).
Axes of the slice: x: 4, y: 8, z: 12 (z_hi: 2, z_lo: 6; z = z_hi * 6 + z_lo), core: 2. Of those that a mesh axis runs over, the one named last changes fastest.
Arguments:
- state: float32 [768, 4, 2, 128, 128], P(('face', 'tile')), may hold values from -3 to 3
- forcing: float32 [768, 2, 4, 128, 128], P(('face', 'tile')), may hold values from -3 to 3
- cotangent: float32 [768, 4, 2, 128, 128], P(('face', 'tile')), may hold values from -6 to 6
- neighbour: int32 [768, 4], P(('face', 'tile')), may hold values from -1 to 767, as said below
- rotation: int32 [768, 4], P(('face', 'tile')), may hold values from 0 to 7
- wet: int32 [768], P(('face', 'tile')), may hold values from 0 to 1, as said below
- levels: int32 [768, 128, 128], P(('face', 'tile')), may hold values from 0 to 2
Outputs:
- state_gradient: float32 [768, 4, 2, 128, 128], P(('face', 'tile'))
- forcing_gradient: float32 [768, 2, 4, 128, 128], P(('face', 'tile'))
The draws below stay inside these ranges and needn't reach their ends.
Inputs may be any that keep to these rules, and one draw needn't show every extreme that they name: The west neighbour of every tile is the tile of the same slot on the device with the same tile index at face index one below (wrapping around the face axis), the east neighbour the one at face index one above; south and north neighbours lie on a device of the same face block or are -1. Every tile on a device of tile index 0 is wet.
All inputs are finite; a program needn't handle non-finite values.
Results may differ from the reference program's by a relative error of at most 0.00005.
Values sent between devices are 32-bit elements; how exact they have to be, the bound alone decides.
No kernel may reach another device: no remote copies, remote signals or barrier semaphores. Data moves between devices by JAX's collectives and lax.ppermute only.
A program may use at most 32 MiB of HBM per device.

```python
import jax
import jax.numpy as jnp

FIELDS = 4
LEVELS = 2
TSIDE = 128
SLOTS = 1
STEPS = 2
FACE_ROWS = 96
GROUP = 8
NTILES = 768


def draw_neighbour(key, part):
    ids = jnp.arange(NTILES, dtype=jnp.int32)[:, None]
    device = ids // SLOTS
    own_slot = ids % SLOTS
    face_idx = device // GROUP
    tile_idx = device % GROUP
    key_kind, key_tile, key_slot = jax.random.split(key, 3)
    kind = jax.random.randint(key_kind, (NTILES, 4), 0, 5, dtype=jnp.int32)
    other_tile = jax.random.randint(key_tile, (NTILES, 4), 0, GROUP, dtype=jnp.int32)
    slot = jax.random.randint(key_slot, (NTILES, 4), 0, SLOTS, dtype=jnp.int32)
    lower = (face_idx + FACE_ROWS - 1) % FACE_ROWS
    upper = (face_idx + 1) % FACE_ROWS
    sides = jnp.arange(4, dtype=jnp.int32)[None, :]
    across_low = (lower * GROUP + tile_idx) * SLOTS + own_slot
    across_high = (upper * GROUP + tile_idx) * SLOTS + own_slot
    inside = (face_idx * GROUP + other_tile) * SLOTS + slot
    inside = jnp.where(kind == 0, -1, inside)
    result = jnp.where(sides == 0, across_low, jnp.where(sides == 1, across_high, inside))
    return result.astype(jnp.int32)


def draw_wet(key, part):
    ids = jnp.arange(NTILES, dtype=jnp.int32)
    tile_idx = ids // SLOTS % GROUP
    pick = jax.random.randint(key, (NTILES,), 0, 4, dtype=jnp.int32)
    return jnp.where((tile_idx == 0) | (pick < 3), 1, 0).astype(jnp.int32)


def set_ends(array, key, low, largest):
    longest = array.shape.index(max(array.shape))
    spots = []
    for shift in (0, 1):
        where = [jax.random.randint(jax.random.fold_in(key, axis), (), 0, length) for axis, length in enumerate(array.shape)]
        where[longest] = (where[longest] + shift) % array.shape[longest]
        spots.append(tuple(where))
    return array.at[spots[0]].set(low).at[spots[1]].set(largest)


def block_levels(key, extent, cuts, smallest, high):
    gain, own = 1.0, jax.random.fold_in(key, 6)
    for axis_at, parts in cuts:
        heights = jnp.exp(jax.random.uniform(jax.random.fold_in(own, axis_at), (parts,), jnp.float32, smallest / len(cuts), high / len(cuts)))
        gain = gain * jnp.repeat(heights, extent[axis_at] // parts).reshape([-1 if axis == axis_at else 1 for axis in range(len(extent))])
    return gain


def gaussian(own_key, extent, deviation, bound, cuts=(), held_as=jnp.bfloat16):
    loudness = block_levels(own_key, extent, cuts, -0.22, 0.18) if cuts else 1.0
    entries = jax.random.normal(own_key, extent, jnp.float32) * deviation * loudness
    return jnp.minimum(jnp.maximum(entries, -bound), bound).astype(held_as)


def setup_inputs(seed: int = 0) -> dict:
    keys = jax.random.split(jax.random.key(seed), 8)
    state = gaussian(keys[0], (NTILES, FIELDS, LEVELS, TSIDE, TSIDE), 0.5, 3.0, ((0, 768),), jnp.float32)
    forcing = gaussian(keys[1], (NTILES, STEPS, FIELDS, TSIDE, TSIDE), 0.5, 3.0, ((0, 768),), jnp.float32)
    cotangent = gaussian(keys[2], (NTILES, FIELDS, LEVELS, TSIDE, TSIDE), 1.0, 6.0, ((0, 768),), jnp.float32)
    neighbour = draw_neighbour(jax.random.fold_in(keys[7], 71), 0)
    rotation = set_ends(jax.random.randint(keys[4], (NTILES, 4), 0, 8), jax.random.fold_in(keys[4], 1), 0, 7).astype(jnp.int32)
    wet = draw_wet(jax.random.fold_in(keys[7], 71), 0)
    levels = set_ends(jax.random.randint(keys[6], (NTILES, TSIDE, TSIDE), 0, LEVELS + 1), jax.random.fold_in(keys[6], 1), 0, LEVELS).astype(jnp.int32)
    return dict(state=state, forcing=forcing, cotangent=cotangent, neighbour=neighbour, rotation=rotation, wet=wet, levels=levels)


time_step = 1.0
diffuse_rate = 0.15
viscosity = 0.15
vertical_mix = 0.1
coriolis = 0.3
buoyancy_scale = 0.25
thermal_coef = 1.0
haline_coef = 0.8
drag_rate = 0.05

def edge_strips(field):
    return jnp.stack([field[..., :, 0], field[..., :, -1], field[..., 0, :], field[..., -1, :]], axis=1)

def place_halo(field, halos):
    padded = jnp.pad(field, ((0, 0), (0, 0), (0, 0), (1, 1), (1, 1)))
    padded = padded.at[..., 1:-1, 0].set(halos[:, 0])
    padded = padded.at[..., 1:-1, -1].set(halos[:, 1])
    padded = padded.at[..., 0, 1:-1].set(halos[:, 2])
    padded = padded.at[..., -1, 1:-1].set(halos[:, 3])
    return padded

def level_mix(values):
    above = jnp.concatenate([values[:, :1], values[:, :-1]], axis=1)
    below = jnp.concatenate([values[:, 1:], values[:, -1:]], axis=1)
    return above + below - 2.0 * values

def step_tiles(padded, mask, drive):
    centre = padded[..., 1:-1, 1:-1]
    east = padded[..., 1:-1, 2:]
    west = padded[..., 1:-1, :-2]
    north = padded[..., 2:, 1:-1]
    south = padded[..., :-2, 1:-1]
    laplace = east + west + north + south - 4.0 * centre
    grad_x = 0.5 * (east - west)
    grad_y = 0.5 * (north - south)
    theta = centre[:, 0]
    salt = centre[:, 1]
    uvel = centre[:, 2]
    vvel = centre[:, 3]
    dens_x = -thermal_coef * grad_x[:, 0] + haline_coef * grad_x[:, 1]
    dens_y = -thermal_coef * grad_y[:, 0] + haline_coef * grad_y[:, 1]
    new_theta = theta + time_step * (-(uvel * grad_x[:, 0] + vvel * grad_y[:, 0]) + diffuse_rate * laplace[:, 0] + vertical_mix * level_mix(theta))
    new_salt = salt + time_step * (-(uvel * grad_x[:, 1] + vvel * grad_y[:, 1]) + diffuse_rate * laplace[:, 1] + vertical_mix * level_mix(salt))
    new_u = uvel + time_step * (viscosity * laplace[:, 2] + coriolis * vvel - buoyancy_scale * dens_x - drag_rate * uvel)
    new_v = vvel + time_step * (viscosity * laplace[:, 3] - coriolis * uvel - buoyancy_scale * dens_y - drag_rate * vvel)
    result = jnp.stack([new_theta, new_salt, new_u, new_v], axis=1)
    result = result.at[:, :, 0].add(time_step * drive)
    return result * mask[:, None]

def fill_halo(field, neighbour, rotation):
    strips = edge_strips(field)
    valid = neighbour >= 0
    source = jnp.maximum(neighbour, 0).astype(jnp.int32)
    side = (rotation % 4).astype(jnp.int32)
    flip = rotation // 4
    chosen = strips[source, side]
    flipped = jnp.where((flip == 1)[..., None, None, None], chosen[..., ::-1], chosen)
    halos = jnp.where(valid[..., None, None, None], flipped, jnp.zeros_like(flipped))
    return place_halo(field, halos)

def reference(state, forcing, cotangent, neighbour, rotation, wet, levels):
    depth = jnp.arange(LEVELS, dtype=jnp.int32)[None, :, None, None]
    mask = ((depth < levels[:, None]) & (wet[:, None, None, None] == 1)).astype(jnp.float32)

    def forward(start, drive):
        field = start * mask[:, None]
        for moment in range(STEPS):
            field = step_tiles(fill_halo(field, neighbour, rotation), mask, drive[:, moment])
        return field
    final_state, pullback = jax.vjp(forward, state, forcing)
    state_gradient, forcing_gradient = pullback(cotangent)
    return (state_gradient, forcing_gradient)
```

```python
import jax
import jax.numpy as jnp
from jax import lax
from jax.sharding import PartitionSpec as P

time_step = 1.0
diffuse_rate = 0.15
viscosity = 0.15
vertical_mix = 0.1
coriolis = 0.3
buoyancy_scale = 0.25
thermal_coef = 1.0
haline_coef = 0.8
drag_rate = 0.05


def with_halo(block, sides, width):
    for axis, dim in sides:
        count = lax.axis_size(axis)
        forward = [(i, i + 1) for i in range(count - 1)]
        forward.append((count - 1, 0))
        backward = [(target, source) for source, target in forward]
        low = lax.ppermute(
            lax.slice_in_dim(block, block.shape[dim] - width, None, axis=dim), axis, forward
        )
        high = lax.ppermute(lax.slice_in_dim(block, 0, width, axis=dim), axis, backward)
        block = jnp.concatenate([low, block, high], axis=dim)
    return block


def edge_strips(field):
    return jnp.stack(
        [field[..., :, 0], field[..., :, -1], field[..., 0, :], field[..., -1, :]], axis=1
    )


def place_halo(field, halos):
    padded = jnp.pad(field, ((0, 0), (0, 0), (0, 0), (1, 1), (1, 1)))
    padded = padded.at[..., 1:-1, 0].set(halos[:, 0])
    padded = padded.at[..., 1:-1, -1].set(halos[:, 1])
    padded = padded.at[..., 0, 1:-1].set(halos[:, 2])
    padded = padded.at[..., -1, 1:-1].set(halos[:, 3])
    return padded


def level_mix(values):
    above = jnp.concatenate([values[:, :1], values[:, :-1]], axis=1)
    below = jnp.concatenate([values[:, 1:], values[:, -1:]], axis=1)
    return above + below - 2.0 * values


def step_tiles(padded, mask, drive):
    centre = padded[..., 1:-1, 1:-1]
    east = padded[..., 1:-1, 2:]
    west = padded[..., 1:-1, :-2]
    north = padded[..., 2:, 1:-1]
    south = padded[..., :-2, 1:-1]
    laplace = east + west + north + south - 4.0 * centre
    grad_x = 0.5 * (east - west)
    grad_y = 0.5 * (north - south)
    theta = centre[:, 0]
    salt = centre[:, 1]
    uvel = centre[:, 2]
    vvel = centre[:, 3]
    dens_x = -thermal_coef * grad_x[:, 0] + haline_coef * grad_x[:, 1]
    dens_y = -thermal_coef * grad_y[:, 0] + haline_coef * grad_y[:, 1]
    new_theta = theta + time_step * (
        -(uvel * grad_x[:, 0] + vvel * grad_y[:, 0])
        + diffuse_rate * laplace[:, 0]
        + vertical_mix * level_mix(theta)
    )
    new_salt = salt + time_step * (
        -(uvel * grad_x[:, 1] + vvel * grad_y[:, 1])
        + diffuse_rate * laplace[:, 1]
        + vertical_mix * level_mix(salt)
    )
    new_u = uvel + time_step * (
        viscosity * laplace[:, 2] + coriolis * vvel - buoyancy_scale * dens_x - drag_rate * uvel
    )
    new_v = vvel + time_step * (
        viscosity * laplace[:, 3] - coriolis * uvel - buoyancy_scale * dens_y - drag_rate * vvel
    )
    result = jnp.stack([new_theta, new_salt, new_u, new_v], axis=1)
    result = result.at[:, :, 0].add(time_step * drive)
    return result * mask[:, None]


def shards(state, forcing, cotangent, neighbour, rotation, wet, levels):
    slot_count = state.shape[0]
    group_size = lax.axis_size("tile")
    face_count = lax.axis_size("face")
    face_index = lax.axis_index("face")
    depth = jnp.arange(state.shape[2], dtype=jnp.int32)[None, :, None, None]
    mask = ((depth < levels[:, None]) & (wet[:, None, None, None] == 1)).astype(jnp.float32)
    valid = neighbour >= 0
    source = jnp.maximum(neighbour, 0)
    device_of = source // slot_count
    slot_of = source % slot_count
    source_face = device_of // group_size
    source_tile = device_of % group_size
    side = rotation % 4
    flip = rotation // 4
    lower_face = (face_index + face_count - 1) % face_count
    tile_index = lax.axis_index("tile")
    block = jnp.where(
        source_face == face_index,
        (tile_index - source_tile) % group_size,
        jnp.where(source_face == lower_face, group_size, group_size + 1),
    )
    column = (block * slot_count + slot_of) * 4 + side
    total = (group_size + 2) * slot_count * 4
    selector = (
        (column[..., None] == jnp.arange(total, dtype=jnp.int32)) & valid[..., None]
    ).astype(jnp.float32)
    selector = selector.reshape(slot_count * 4, total)
    reverse = (flip == 1)[..., None, None, None]

    def shift_tile(x, k):
        pairs = [(i, (i + k) % group_size) for i in range(group_size)]
        return lax.ppermute(x, "tile", pairs)

    def gather_rims(field):
        strips = edge_strips(field)[None]
        grouped = [strips] + [shift_tile(strips, k) for k in range(1, group_size)]
        beside_all = with_halo(strips, (("face", 0),), 1)
        return jnp.concatenate(grouped + [beside_all[0:1], beside_all[2:3]], axis=0)

    def assemble(field, candidates):
        flat = candidates.reshape(total, -1)
        chosen = jnp.dot(selector, flat, precision=lax.Precision.HIGHEST)
        chosen = chosen.reshape(slot_count, 4, field.shape[1], field.shape[2], field.shape[3])
        flipped = jnp.where(reverse, chosen[..., ::-1], chosen)
        return place_halo(field, flipped)

    def fill(field):
        return assemble(field, gather_rims(field))

    def fill_back(ct_padded, field):
        cand_shape = (group_size + 2, slot_count, 4, field.shape[1], field.shape[2], field.shape[3])
        blank_cands = jnp.zeros(cand_shape, jnp.float32)
        unused, pull_assemble = jax.vjp(assemble, jnp.zeros_like(field), blank_cands)
        ct_field, ct_cands = pull_assemble(ct_padded)
        back_group = ct_cands[0:1]
        for k in range(1, group_size):
            back_group = back_group + shift_tile(ct_cands[k : k + 1], -k)
        back_face = with_halo(ct_cands[group_size:], (("face", 0),), 1)
        ct_strips = back_group[0] + back_face[0] + back_face[3]
        unused_edges, pull_edges = jax.vjp(edge_strips, jnp.zeros_like(field))
        (extra,) = pull_edges(ct_strips)
        return ct_field + extra

    def stepper(padded, drive):
        return step_tiles(padded, mask, drive)

    first = state * mask[:, None]
    padded_first = fill(first)
    second = step_tiles(padded_first, mask, forcing[:, 0])
    padded_second = fill(second)
    unused_a, pull_second = jax.vjp(stepper, padded_second, forcing[:, 1])
    ct_pad_second, ct_drive_second = pull_second(cotangent)
    ct_second = fill_back(ct_pad_second, second)
    unused_b, pull_first = jax.vjp(stepper, padded_first, forcing[:, 0])
    ct_pad_first, ct_drive_first = pull_first(ct_second)
    ct_first = fill_back(ct_pad_first, first)
    state_gradient = ct_first * mask[:, None]
    forcing_gradient = jnp.stack([ct_drive_first, ct_drive_second], axis=1)
    return (state_gradient, forcing_gradient)


def solution(mesh):
    placed = (
        P(("face", "tile"), None, None, None, None),
        P(("face", "tile"), None, None, None, None),
        P(("face", "tile"), None, None, None, None),
        P(("face", "tile"), None),
        P(("face", "tile"), None),
        P(("face", "tile")),
        P(("face", "tile"), None, None),
    )
    return jax.shard_map(
        shards,
        mesh=mesh,
        in_specs=placed,
        out_specs=(
            P(("face", "tile"), None, None, None, None),
            P(("face", "tile"), None, None, None, None),
        ),
        check_vma=False,
    )
```

```python
import jax
import jax.numpy as jnp
from jax import lax
from jax.sharding import PartitionSpec as P

time_step = 1.0
diffuse_rate = 0.15
viscosity = 0.15
vertical_mix = 0.1
coriolis = 0.3
buoyancy_scale = 0.25
thermal_coef = 1.0
haline_coef = 0.8
drag_rate = 0.05


def with_halo(block, sides, width):
    for axis, dim in sides:
        count = lax.axis_size(axis)
        forward = [(i, i + 1) for i in range(count - 1)]
        forward.append((count - 1, 0))
        backward = [(target, source) for source, target in forward]
        low = lax.ppermute(
            lax.slice_in_dim(block, block.shape[dim] - width, None, axis=dim), axis, forward
        )
        high = lax.ppermute(lax.slice_in_dim(block, 0, width, axis=dim), axis, backward)
        block = jnp.concatenate([low, block, high], axis=dim)
    return block


def edge_strips(field):
    return jnp.stack(
        [field[..., :, 0], field[..., :, -1], field[..., 0, :], field[..., -1, :]], axis=1
    )


def place_halo(field, halos):
    padded = jnp.pad(field, ((0, 0), (0, 0), (0, 0), (1, 1), (1, 1)))
    padded = padded.at[..., 1:-1, 0].set(halos[:, 0])
    padded = padded.at[..., 1:-1, -1].set(halos[:, 1])
    padded = padded.at[..., 0, 1:-1].set(halos[:, 2])
    padded = padded.at[..., -1, 1:-1].set(halos[:, 3])
    return padded


def level_mix(values):
    above = jnp.concatenate([values[:, :1], values[:, :-1]], axis=1)
    below = jnp.concatenate([values[:, 1:], values[:, -1:]], axis=1)
    return above + below - 2.0 * values


def step_tiles(padded, mask, drive):
    centre = padded[..., 1:-1, 1:-1]
    east = padded[..., 1:-1, 2:]
    west = padded[..., 1:-1, :-2]
    north = padded[..., 2:, 1:-1]
    south = padded[..., :-2, 1:-1]
    laplace = east + west + north + south - 4.0 * centre
    grad_x = 0.5 * (east - west)
    grad_y = 0.5 * (north - south)
    theta = centre[:, 0]
    salt = centre[:, 1]
    uvel = centre[:, 2]
    vvel = centre[:, 3]
    dens_x = -thermal_coef * grad_x[:, 0] + haline_coef * grad_x[:, 1]
    dens_y = -thermal_coef * grad_y[:, 0] + haline_coef * grad_y[:, 1]
    new_theta = theta + time_step * (
        -(uvel * grad_x[:, 0] + vvel * grad_y[:, 0])
        + diffuse_rate * laplace[:, 0]
        + vertical_mix * level_mix(theta)
    )
    new_salt = salt + time_step * (
        -(uvel * grad_x[:, 1] + vvel * grad_y[:, 1])
        + diffuse_rate * laplace[:, 1]
        + vertical_mix * level_mix(salt)
    )
    new_u = uvel + time_step * (
        viscosity * laplace[:, 2] + coriolis * vvel - buoyancy_scale * dens_x - drag_rate * uvel
    )
    new_v = vvel + time_step * (
        viscosity * laplace[:, 3] - coriolis * uvel - buoyancy_scale * dens_y - drag_rate * vvel
    )
    result = jnp.stack([new_theta, new_salt, new_u, new_v], axis=1)
    result = result.at[:, :, 0].add(time_step * drive)
    return result * mask[:, None]


def shards(state, forcing, cotangent, neighbour, rotation, wet, levels):
    slot_count = state.shape[0]
    group_size = lax.axis_size("tile")
    face_count = lax.axis_size("face")
    face_index = lax.axis_index("face")
    depth = jnp.arange(state.shape[2], dtype=jnp.int32)[None, :, None, None]
    mask = ((depth < levels[:, None]) & (wet[:, None, None, None] == 1)).astype(jnp.float32)
    valid = neighbour >= 0
    source = jnp.maximum(neighbour, 0)
    device_of = source // slot_count
    slot_of = source % slot_count
    source_face = device_of // group_size
    source_tile = device_of % group_size
    side = rotation % 4
    flip = rotation // 4
    lower_face = (face_index + face_count - 1) % face_count
    block = jnp.where(
        source_face == face_index,
        source_tile,
        jnp.where(source_face == lower_face, group_size, group_size + 1),
    )
    column = (block * slot_count + slot_of) * 4 + side
    total = (group_size + 2) * slot_count * 4
    selector = (
        (column[..., None] == jnp.arange(total, dtype=jnp.int32)) & valid[..., None]
    ).astype(jnp.float32)
    selector = selector.reshape(slot_count * 4, total)
    reverse = (flip == 1)[..., None, None, None]

    def gather_rims(field):
        strips = edge_strips(field)[None]
        copies = jnp.broadcast_to(strips, (group_size,) + strips.shape[1:])
        grouped = lax.all_to_all(copies, "tile", 0, 0, tiled=True)
        beside_all = with_halo(strips, (("face", 0),), 1)
        return jnp.concatenate([grouped, beside_all[0:1], beside_all[2:3]], axis=0)

    def assemble(field, candidates):
        flat = candidates.reshape(total, -1)
        chosen = jnp.dot(selector, flat, precision=lax.Precision.HIGHEST)
        chosen = chosen.reshape(slot_count, 4, field.shape[1], field.shape[2], field.shape[3])
        flipped = jnp.where(reverse, chosen[..., ::-1], chosen)
        return place_halo(field, flipped)

    def fill(field):
        return assemble(field, gather_rims(field))

    def fill_back(ct_padded, field):
        cand_shape = (group_size + 2, slot_count, 4, field.shape[1], field.shape[2], field.shape[3])
        blank_cands = jnp.zeros(cand_shape, jnp.float32)
        unused, pull_assemble = jax.vjp(assemble, jnp.zeros_like(field), blank_cands)
        ct_field, ct_cands = pull_assemble(ct_padded)
        returned = lax.all_to_all(ct_cands[:group_size], "tile", 0, 0, tiled=True)
        back_group = jnp.sum(returned, axis=0, keepdims=True)
        back_face = with_halo(ct_cands[group_size:], (("face", 0),), 1)
        ct_strips = back_group[0] + back_face[0] + back_face[3]
        unused_edges, pull_edges = jax.vjp(edge_strips, jnp.zeros_like(field))
        (extra,) = pull_edges(ct_strips)
        return ct_field + extra

    def stepper(padded, drive):
        return step_tiles(padded, mask, drive)

    first = state * mask[:, None]
    padded_first = fill(first)
    second = step_tiles(padded_first, mask, forcing[:, 0])
    padded_second = fill(second)
    unused_a, pull_second = jax.vjp(stepper, padded_second, forcing[:, 1])
    ct_pad_second, ct_drive_second = pull_second(cotangent)
    ct_second = fill_back(ct_pad_second, second)
    unused_b, pull_first = jax.vjp(stepper, padded_first, forcing[:, 0])
    ct_pad_first, ct_drive_first = pull_first(ct_second)
    ct_first = fill_back(ct_pad_first, first)
    state_gradient = ct_first * mask[:, None]
    forcing_gradient = jnp.stack([ct_drive_first, ct_drive_second], axis=1)
    return (state_gradient, forcing_gradient)


def solution(mesh):
    placed = (
        P(("face", "tile"), None, None, None, None),
        P(("face", "tile"), None, None, None, None),
        P(("face", "tile"), None, None, None, None),
        P(("face", "tile"), None),
        P(("face", "tile"), None),
        P(("face", "tile")),
        P(("face", "tile"), None, None),
    )
    return jax.shard_map(
        shards,
        mesh=mesh,
        in_specs=placed,
        out_specs=(
            P(("face", "tile"), None, None, None, None),
            P(("face", "tile"), None, None, None, None),
        ),
        check_vma=False,
    )
```

```python
import jax
import jax.numpy as jnp
from jax import lax
from jax.sharding import PartitionSpec as P

time_step = 1.0
diffuse_rate = 0.15
viscosity = 0.15
vertical_mix = 0.1
coriolis = 0.3
buoyancy_scale = 0.25
thermal_coef = 1.0
haline_coef = 0.8
drag_rate = 0.05


def with_halo(block, sides, width):
    for axis, dim in sides:
        count = lax.axis_size(axis)
        forward = [(i, i + 1) for i in range(count - 1)]
        forward.append((count - 1, 0))
        backward = [(target, source) for source, target in forward]
        low = lax.ppermute(
            lax.slice_in_dim(block, block.shape[dim] - width, None, axis=dim), axis, forward
        )
        high = lax.ppermute(lax.slice_in_dim(block, 0, width, axis=dim), axis, backward)
        block = jnp.concatenate([low, block, high], axis=dim)
    return block


def edge_strips(field):
    return jnp.stack(
        [field[..., :, 0], field[..., :, -1], field[..., 0, :], field[..., -1, :]], axis=1
    )


def place_halo(field, halos):
    middle = jnp.concatenate([halos[:, 0][..., None], field, halos[:, 1][..., None]], axis=-1)
    corner = jnp.zeros(halos.shape[:1] + halos.shape[2:-1] + (1,), field.dtype)
    south = jnp.concatenate([corner, halos[:, 2], corner], axis=-1)[..., None, :]
    north = jnp.concatenate([corner, halos[:, 3], corner], axis=-1)[..., None, :]
    return jnp.concatenate([south, middle, north], axis=-2)


def level_mix(values):
    above = jnp.concatenate([values[:, :1], values[:, :-1]], axis=1)
    below = jnp.concatenate([values[:, 1:], values[:, -1:]], axis=1)
    return above + below - 2.0 * values


def step_tiles(padded, mask, drive):
    centre = padded[..., 1:-1, 1:-1]
    east = padded[..., 1:-1, 2:]
    west = padded[..., 1:-1, :-2]
    north = padded[..., 2:, 1:-1]
    south = padded[..., :-2, 1:-1]
    laplace = east + west + north + south - 4.0 * centre
    grad_x = 0.5 * (east - west)
    grad_y = 0.5 * (north - south)
    theta = centre[:, 0]
    salt = centre[:, 1]
    uvel = centre[:, 2]
    vvel = centre[:, 3]
    dens_x = -thermal_coef * grad_x[:, 0] + haline_coef * grad_x[:, 1]
    dens_y = -thermal_coef * grad_y[:, 0] + haline_coef * grad_y[:, 1]
    new_theta = theta + time_step * (
        -(uvel * grad_x[:, 0] + vvel * grad_y[:, 0])
        + diffuse_rate * laplace[:, 0]
        + vertical_mix * level_mix(theta)
    )
    new_salt = salt + time_step * (
        -(uvel * grad_x[:, 1] + vvel * grad_y[:, 1])
        + diffuse_rate * laplace[:, 1]
        + vertical_mix * level_mix(salt)
    )
    new_u = uvel + time_step * (
        viscosity * laplace[:, 2] + coriolis * vvel - buoyancy_scale * dens_x - drag_rate * uvel
    )
    new_v = vvel + time_step * (
        viscosity * laplace[:, 3] - coriolis * uvel - buoyancy_scale * dens_y - drag_rate * vvel
    )
    result = jnp.stack([new_theta, new_salt, new_u, new_v], axis=1)
    surface = result[:, :, 0:1] + (time_step * drive)[:, :, None]
    result = jnp.concatenate([surface, result[:, :, 1:]], axis=2)
    return result * mask[:, None]


def shards(state, forcing, cotangent, neighbour, rotation, wet, levels):
    slot_count = state.shape[0]
    group_size = lax.axis_size("tile")
    face_count = lax.axis_size("face")
    face_index = lax.axis_index("face")
    depth = jnp.arange(state.shape[2], dtype=jnp.int32)[None, :, None, None]
    mask = ((depth < levels[:, None]) & (wet[:, None, None, None] == 1)).astype(jnp.float32)
    valid = neighbour >= 0
    source = jnp.maximum(neighbour, 0)
    device_of = source // slot_count
    slot_of = source % slot_count
    source_face = device_of // group_size
    source_tile = device_of % group_size
    side = rotation % 4
    flip = rotation // 4
    lower_face = (face_index + face_count - 1) % face_count
    block = jnp.where(
        source_face == face_index,
        source_tile,
        jnp.where(source_face == lower_face, group_size, group_size + 1),
    )
    column = (block * slot_count + slot_of) * 4 + side
    total = (group_size + 2) * slot_count * 4
    selector = (
        (column[..., None] == jnp.arange(total, dtype=jnp.int32)) & valid[..., None]
    ).astype(jnp.float32)
    selector = selector.reshape(slot_count * 4, total)
    reverse = (flip == 1)[..., None, None, None]

    def gather_rims(field):
        strips = edge_strips(field)[None]
        copies = jnp.broadcast_to(strips, (group_size,) + strips.shape[1:])
        grouped = lax.all_to_all(copies, "tile", 0, 0, tiled=True)
        beside_all = with_halo(strips, (("face", 0),), 1)
        return jnp.concatenate([grouped, beside_all[0:1], beside_all[2:3]], axis=0)

    def assemble(field, candidates):
        flat = candidates.reshape(total, -1)
        chosen = jnp.dot(selector, flat, precision=lax.Precision.HIGHEST)
        chosen = chosen.reshape(slot_count, 4, field.shape[1], field.shape[2], field.shape[3])
        flipped = jnp.where(reverse, chosen[..., ::-1], chosen)
        return place_halo(field, flipped)

    def fill(field):
        return assemble(field, gather_rims(field))

    def fill_back(ct_padded, field):
        cand_shape = (group_size + 2, slot_count, 4, field.shape[1], field.shape[2], field.shape[3])
        blank_cands = jnp.zeros(cand_shape, jnp.float32)
        unused, pull_assemble = jax.vjp(assemble, jnp.zeros_like(field), blank_cands)
        ct_field, ct_cands = pull_assemble(ct_padded)
        returned = lax.all_to_all(ct_cands[:group_size], "tile", 0, 0, tiled=True)
        back_group = jnp.sum(returned, axis=0, keepdims=True)
        back_face = with_halo(ct_cands[group_size:], (("face", 0),), 1)
        ct_strips = back_group[0] + back_face[0] + back_face[3]
        unused_edges, pull_edges = jax.vjp(edge_strips, jnp.zeros_like(field))
        (extra,) = pull_edges(ct_strips)
        return ct_field + extra

    def stepper(padded, drive):
        return step_tiles(padded, mask, drive)

    first = state * mask[:, None]
    padded_first = fill(first)
    second = step_tiles(padded_first, mask, forcing[:, 0])
    padded_second = fill(second)
    unused_a, pull_second = jax.vjp(stepper, padded_second, forcing[:, 1])
    ct_pad_second, ct_drive_second = pull_second(cotangent)
    ct_second = fill_back(ct_pad_second, second)
    unused_b, pull_first = jax.vjp(stepper, padded_first, forcing[:, 0])
    ct_pad_first, ct_drive_first = pull_first(ct_second)
    ct_first = fill_back(ct_pad_first, first)
    state_gradient = ct_first * mask[:, None]
    forcing_gradient = jnp.stack([ct_drive_first, ct_drive_second], axis=1)
    return (state_gradient, forcing_gradient)


def solution(mesh):
    placed = (
        P(("face", "tile"), None, None, None, None),
        P(("face", "tile"), None, None, None, None),
        P(("face", "tile"), None, None, None, None),
        P(("face", "tile"), None),
        P(("face", "tile"), None),
        P(("face", "tile")),
        P(("face", "tile"), None, None),
    )
    return jax.shard_map(
        shards,
        mesh=mesh,
        in_specs=placed,
        out_specs=(
            P(("face", "tile"), None, None, None, None),
            P(("face", "tile"), None, None, None, None),
        ),
        check_vma=False,
    )
```

```python
import jax
import jax.numpy as jnp
from jax import lax
from jax.sharding import PartitionSpec as P

time_step = 1.0
diffuse_rate = 0.15
viscosity = 0.15
vertical_mix = 0.1
coriolis = 0.3
buoyancy_scale = 0.25
thermal_coef = 1.0
haline_coef = 0.8
drag_rate = 0.05


def with_halo(block, sides, width):
    for axis, dim in sides:
        count = lax.axis_size(axis)
        forward = [(i, i + 1) for i in range(count - 1)]
        forward.append((count - 1, 0))
        backward = [(target, source) for source, target in forward]
        low = lax.ppermute(
            lax.slice_in_dim(block, block.shape[dim] - width, None, axis=dim), axis, forward
        )
        high = lax.ppermute(lax.slice_in_dim(block, 0, width, axis=dim), axis, backward)
        block = jnp.concatenate([low, block, high], axis=dim)
    return block


def edge_strips(field):
    return jnp.stack(
        [field[..., :, 0], field[..., :, -1], field[..., 0, :], field[..., -1, :]], axis=1
    )


def level_mix(values):
    above = jnp.concatenate([values[:, :1], values[:, :-1]], axis=1)
    below = jnp.concatenate([values[:, 1:], values[:, -1:]], axis=1)
    return above + below - 2.0 * values


def step_tiles(centre, halos, mask, drive):
    east = jnp.concatenate([centre[..., :, 1:], halos[:, 1][..., :, None]], axis=-1)
    west = jnp.concatenate([halos[:, 0][..., :, None], centre[..., :, :-1]], axis=-1)
    north = jnp.concatenate([centre[..., 1:, :], halos[:, 3][..., None, :]], axis=-2)
    south = jnp.concatenate([halos[:, 2][..., None, :], centre[..., :-1, :]], axis=-2)
    laplace = east + west + north + south - 4.0 * centre
    grad_x = 0.5 * (east - west)
    grad_y = 0.5 * (north - south)
    theta = centre[:, 0]
    salt = centre[:, 1]
    uvel = centre[:, 2]
    vvel = centre[:, 3]
    dens_x = -thermal_coef * grad_x[:, 0] + haline_coef * grad_x[:, 1]
    dens_y = -thermal_coef * grad_y[:, 0] + haline_coef * grad_y[:, 1]
    new_theta = theta + time_step * (
        -(uvel * grad_x[:, 0] + vvel * grad_y[:, 0])
        + diffuse_rate * laplace[:, 0]
        + vertical_mix * level_mix(theta)
    )
    new_salt = salt + time_step * (
        -(uvel * grad_x[:, 1] + vvel * grad_y[:, 1])
        + diffuse_rate * laplace[:, 1]
        + vertical_mix * level_mix(salt)
    )
    new_u = uvel + time_step * (
        viscosity * laplace[:, 2] + coriolis * vvel - buoyancy_scale * dens_x - drag_rate * uvel
    )
    new_v = vvel + time_step * (
        viscosity * laplace[:, 3] - coriolis * uvel - buoyancy_scale * dens_y - drag_rate * vvel
    )
    result = jnp.stack([new_theta, new_salt, new_u, new_v], axis=1)
    surface = result[:, :, 0:1] + (time_step * drive)[:, :, None]
    result = jnp.concatenate([surface, result[:, :, 1:]], axis=2)
    return result * mask[:, None]


def shards(state, forcing, cotangent, neighbour, rotation, wet, levels):
    slot_count = state.shape[0]
    group_size = lax.axis_size("tile")
    face_count = lax.axis_size("face")
    face_index = lax.axis_index("face")
    depth = jnp.arange(state.shape[2], dtype=jnp.int32)[None, :, None, None]
    mask = ((depth < levels[:, None]) & (wet[:, None, None, None] == 1)).astype(jnp.float32)
    valid = neighbour >= 0
    source = jnp.maximum(neighbour, 0)
    device_of = source // slot_count
    slot_of = source % slot_count
    source_face = device_of // group_size
    source_tile = device_of % group_size
    side = rotation % 4
    flip = rotation // 4
    lower_face = (face_index + face_count - 1) % face_count
    block = jnp.where(
        source_face == face_index,
        source_tile,
        jnp.where(source_face == lower_face, group_size, group_size + 1),
    )
    column = (block * slot_count + slot_of) * 4 + side
    total = (group_size + 2) * slot_count * 4
    selector = (
        (column[..., None] == jnp.arange(total, dtype=jnp.int32)) & valid[..., None]
    ).astype(jnp.float32)
    selector = selector.reshape(slot_count * 4, total)
    reverse = (flip == 1)[..., None, None, None]

    def gather_rims(field):
        strips = edge_strips(field)[None]
        copies = jnp.broadcast_to(strips, (group_size,) + strips.shape[1:])
        grouped = lax.all_to_all(copies, "tile", 0, 0, tiled=True)
        beside_all = with_halo(strips, (("face", 0),), 1)
        return jnp.concatenate([grouped, beside_all[0:1], beside_all[2:3]], axis=0)

    def assemble(field, candidates):
        flat = candidates.reshape(total, -1)
        chosen = jnp.dot(selector, flat, precision=lax.Precision.HIGHEST)
        chosen = chosen.reshape(slot_count, 4, field.shape[1], field.shape[2], field.shape[3])
        return jnp.where(reverse, chosen[..., ::-1], chosen)

    def fill(field):
        return assemble(field, gather_rims(field))

    def fill_back(ct_halos, field):
        cand_shape = (group_size + 2, slot_count, 4, field.shape[1], field.shape[2], field.shape[3])
        blank_cands = jnp.zeros(cand_shape, jnp.float32)
        unused, pull_assemble = jax.vjp(lambda c: assemble(field, c), blank_cands)
        (ct_cands,) = pull_assemble(ct_halos)
        returned = lax.all_to_all(ct_cands[:group_size], "tile", 0, 0, tiled=True)
        back_group = jnp.sum(returned, axis=0, keepdims=True)
        back_face = with_halo(ct_cands[group_size:], (("face", 0),), 1)
        ct_strips = back_group[0] + back_face[0] + back_face[3]
        unused_edges, pull_edges = jax.vjp(edge_strips, jnp.zeros_like(field))
        (extra,) = pull_edges(ct_strips)
        return extra

    def stepper(field, halos, drive):
        return step_tiles(field, halos, mask, drive)

    first = state * mask[:, None]
    halos_first = fill(first)
    second = step_tiles(first, halos_first, mask, forcing[:, 0])
    halos_second = fill(second)
    unused_a, pull_second = jax.vjp(stepper, second, halos_second, forcing[:, 1])
    ct_local_second, ct_halo_second, ct_drive_second = pull_second(cotangent)
    ct_second = ct_local_second + fill_back(ct_halo_second, second)
    unused_b, pull_first = jax.vjp(stepper, first, halos_first, forcing[:, 0])
    ct_local_first, ct_halo_first, ct_drive_first = pull_first(ct_second)
    ct_first = ct_local_first + fill_back(ct_halo_first, first)
    state_gradient = ct_first * mask[:, None]
    forcing_gradient = jnp.stack([ct_drive_first, ct_drive_second], axis=1)
    return (state_gradient, forcing_gradient)


def solution(mesh):
    placed = (
        P(("face", "tile"), None, None, None, None),
        P(("face", "tile"), None, None, None, None),
        P(("face", "tile"), None, None, None, None),
        P(("face", "tile"), None),
        P(("face", "tile"), None),
        P(("face", "tile")),
        P(("face", "tile"), None, None),
    )
    return jax.shard_map(
        shards,
        mesh=mesh,
        in_specs=placed,
        out_specs=(
            P(("face", "tile"), None, None, None, None),
            P(("face", "tile"), None, None, None, None),
        ),
        check_vma=False,
    )
```

```python
import jax
import jax.numpy as jnp
from jax import lax
from jax.sharding import PartitionSpec as P

time_step = 1.0
diffuse_rate = 0.15
viscosity = 0.15
vertical_mix = 0.1
coriolis = 0.3
buoyancy_scale = 0.25
thermal_coef = 1.0
haline_coef = 0.8
drag_rate = 0.05


def with_halo(block, sides, width):
    for axis, dim in sides:
        count = lax.axis_size(axis)
        forward = [(i, i + 1) for i in range(count - 1)]
        forward.append((count - 1, 0))
        backward = [(target, source) for source, target in forward]
        low = lax.ppermute(
            lax.slice_in_dim(block, block.shape[dim] - width, None, axis=dim), axis, forward
        )
        high = lax.ppermute(lax.slice_in_dim(block, 0, width, axis=dim), axis, backward)
        block = jnp.concatenate([low, block, high], axis=dim)
    return block


def edge_strips(field):
    return jnp.stack(
        [field[..., :, 0], field[..., :, -1], field[..., 0, :], field[..., -1, :]], axis=1
    )


def level_mix(values):
    above = jnp.concatenate([values[:, :1], values[:, :-1]], axis=1)
    below = jnp.concatenate([values[:, 1:], values[:, -1:]], axis=1)
    return above + below - 2.0 * values


def shifted(centre, halo, axis, forward):
    size = centre.shape[axis]
    lead = [(0, 0)] * (centre.ndim - 2)
    if axis == -1:
        inner = centre[..., :, 1:] if forward else centre[..., :, :-1]
        widths = lead + [(0, 0), (0, 1) if forward else (1, 0)]
        spot = lax.broadcasted_iota(jnp.int32, centre.shape, centre.ndim - 1)
        edge = halo[..., :, None]
    else:
        inner = centre[..., 1:, :] if forward else centre[..., :-1, :]
        widths = lead + [(0, 1) if forward else (1, 0), (0, 0)]
        spot = lax.broadcasted_iota(jnp.int32, centre.shape, centre.ndim - 2)
        edge = halo[..., None, :]
    at_edge = spot == (size - 1 if forward else 0)
    return jnp.where(at_edge, edge, jnp.pad(inner, widths))


def step_tiles(centre, halos, mask, drive):
    east = shifted(centre, halos[:, 1], -1, True)
    west = shifted(centre, halos[:, 0], -1, False)
    north = shifted(centre, halos[:, 3], -2, True)
    south = shifted(centre, halos[:, 2], -2, False)
    laplace = east + west + north + south - 4.0 * centre
    grad_x = 0.5 * (east - west)
    grad_y = 0.5 * (north - south)
    theta = centre[:, 0]
    salt = centre[:, 1]
    uvel = centre[:, 2]
    vvel = centre[:, 3]
    dens_x = -thermal_coef * grad_x[:, 0] + haline_coef * grad_x[:, 1]
    dens_y = -thermal_coef * grad_y[:, 0] + haline_coef * grad_y[:, 1]
    new_theta = theta + time_step * (
        -(uvel * grad_x[:, 0] + vvel * grad_y[:, 0])
        + diffuse_rate * laplace[:, 0]
        + vertical_mix * level_mix(theta)
    )
    new_salt = salt + time_step * (
        -(uvel * grad_x[:, 1] + vvel * grad_y[:, 1])
        + diffuse_rate * laplace[:, 1]
        + vertical_mix * level_mix(salt)
    )
    new_u = uvel + time_step * (
        viscosity * laplace[:, 2] + coriolis * vvel - buoyancy_scale * dens_x - drag_rate * uvel
    )
    new_v = vvel + time_step * (
        viscosity * laplace[:, 3] - coriolis * uvel - buoyancy_scale * dens_y - drag_rate * vvel
    )
    result = jnp.stack([new_theta, new_salt, new_u, new_v], axis=1)
    surface = result[:, :, 0:1] + (time_step * drive)[:, :, None]
    result = jnp.concatenate([surface, result[:, :, 1:]], axis=2)
    return result * mask[:, None]


def shards(state, forcing, cotangent, neighbour, rotation, wet, levels):
    slot_count = state.shape[0]
    group_size = lax.axis_size("tile")
    face_count = lax.axis_size("face")
    face_index = lax.axis_index("face")
    depth = jnp.arange(state.shape[2], dtype=jnp.int32)[None, :, None, None]
    mask = ((depth < levels[:, None]) & (wet[:, None, None, None] == 1)).astype(jnp.float32)
    valid = neighbour >= 0
    source = jnp.maximum(neighbour, 0)
    device_of = source // slot_count
    slot_of = source % slot_count
    source_face = device_of // group_size
    source_tile = device_of % group_size
    side = rotation % 4
    flip = rotation // 4
    lower_face = (face_index + face_count - 1) % face_count
    block = jnp.where(
        source_face == face_index,
        source_tile,
        jnp.where(source_face == lower_face, group_size, group_size + 1),
    )
    column = (block * slot_count + slot_of) * 4 + side
    total = (group_size + 2) * slot_count * 4
    selector = (
        (column[..., None] == jnp.arange(total, dtype=jnp.int32)) & valid[..., None]
    ).astype(jnp.float32)
    selector = selector.reshape(slot_count * 4, total)
    reverse = (flip == 1)[..., None, None, None]

    def gather_rims(field):
        strips = edge_strips(field)[None]
        copies = jnp.broadcast_to(strips, (group_size,) + strips.shape[1:])
        grouped = lax.all_to_all(copies, "tile", 0, 0, tiled=True)
        beside_all = with_halo(strips, (("face", 0),), 1)
        return jnp.concatenate([grouped, beside_all[0:1], beside_all[2:3]], axis=0)

    def assemble(field, candidates):
        flat = candidates.reshape(total, -1)
        chosen = jnp.dot(selector, flat, precision=lax.Precision.HIGHEST)
        chosen = chosen.reshape(slot_count, 4, field.shape[1], field.shape[2], field.shape[3])
        return jnp.where(reverse, chosen[..., ::-1], chosen)

    def fill(field):
        return assemble(field, gather_rims(field))

    def fill_back(ct_halos, field):
        cand_shape = (group_size + 2, slot_count, 4, field.shape[1], field.shape[2], field.shape[3])
        blank_cands = jnp.zeros(cand_shape, jnp.float32)
        unused, pull_assemble = jax.vjp(lambda c: assemble(field, c), blank_cands)
        (ct_cands,) = pull_assemble(ct_halos)
        returned = lax.all_to_all(ct_cands[:group_size], "tile", 0, 0, tiled=True)
        back_group = jnp.sum(returned, axis=0, keepdims=True)
        back_face = with_halo(ct_cands[group_size:], (("face", 0),), 1)
        ct_strips = back_group[0] + back_face[0] + back_face[3]
        unused_edges, pull_edges = jax.vjp(edge_strips, jnp.zeros_like(field))
        (extra,) = pull_edges(ct_strips)
        return extra

    def stepper(field, halos, drive):
        return step_tiles(field, halos, mask, drive)

    first = state * mask[:, None]
    halos_first = fill(first)
    second = step_tiles(first, halos_first, mask, forcing[:, 0])
    halos_second = fill(second)
    unused_a, pull_second = jax.vjp(stepper, second, halos_second, forcing[:, 1])
    ct_local_second, ct_halo_second, ct_drive_second = pull_second(cotangent)
    ct_second = ct_local_second + fill_back(ct_halo_second, second)
    unused_b, pull_first = jax.vjp(stepper, first, halos_first, forcing[:, 0])
    ct_local_first, ct_halo_first, ct_drive_first = pull_first(ct_second)
    ct_first = ct_local_first + fill_back(ct_halo_first, first)
    state_gradient = ct_first * mask[:, None]
    forcing_gradient = jnp.stack([ct_drive_first, ct_drive_second], axis=1)
    return (state_gradient, forcing_gradient)


def solution(mesh):
    placed = (
        P(("face", "tile"), None, None, None, None),
        P(("face", "tile"), None, None, None, None),
        P(("face", "tile"), None, None, None, None),
        P(("face", "tile"), None),
        P(("face", "tile"), None),
        P(("face", "tile")),
        P(("face", "tile"), None, None),
    )
    return jax.shard_map(
        shards,
        mesh=mesh,
        in_specs=placed,
        out_specs=(
            P(("face", "tile"), None, None, None, None),
            P(("face", "tile"), None, None, None, None),
        ),
        check_vma=False,
    )
```

```python
import jax
import jax.numpy as jnp
from jax import lax
from jax.sharding import PartitionSpec as P

time_step = 1.0
diffuse_rate = 0.15
viscosity = 0.15
vertical_mix = 0.1
coriolis = 0.3
buoyancy_scale = 0.25
thermal_coef = 1.0
haline_coef = 0.8
drag_rate = 0.05


def with_halo(block, sides, width):
    for axis, dim in sides:
        count = lax.axis_size(axis)
        forward = [(i, i + 1) for i in range(count - 1)]
        forward.append((count - 1, 0))
        backward = [(target, source) for source, target in forward]
        low = lax.ppermute(
            lax.slice_in_dim(block, block.shape[dim] - width, None, axis=dim), axis, forward
        )
        high = lax.ppermute(lax.slice_in_dim(block, 0, width, axis=dim), axis, backward)
        block = jnp.concatenate([low, block, high], axis=dim)
    return block


def edge_strips(field):
    return jnp.stack(
        [field[..., :, 0], field[..., :, -1], field[..., 0, :], field[..., -1, :]], axis=1
    )


def level_mix(values):
    above = jnp.concatenate([values[:, :1], values[:, :-1]], axis=1)
    below = jnp.concatenate([values[:, 1:], values[:, -1:]], axis=1)
    return above + below - 2.0 * values


def step_tiles(centre, halos, mask, drive):
    east = jnp.concatenate([centre[..., :, 1:], halos[:, 1][..., :, None]], axis=-1)
    west = jnp.concatenate([halos[:, 0][..., :, None], centre[..., :, :-1]], axis=-1)
    north = jnp.concatenate([centre[..., 1:, :], halos[:, 3][..., None, :]], axis=-2)
    south = jnp.concatenate([halos[:, 2][..., None, :], centre[..., :-1, :]], axis=-2)
    laplace = east + west + north + south - 4.0 * centre
    grad_x = 0.5 * (east - west)
    grad_y = 0.5 * (north - south)
    theta = centre[:, 0]
    salt = centre[:, 1]
    uvel = centre[:, 2]
    vvel = centre[:, 3]
    dens_x = -thermal_coef * grad_x[:, 0] + haline_coef * grad_x[:, 1]
    dens_y = -thermal_coef * grad_y[:, 0] + haline_coef * grad_y[:, 1]
    new_theta = theta + time_step * (
        -(uvel * grad_x[:, 0] + vvel * grad_y[:, 0])
        + diffuse_rate * laplace[:, 0]
        + vertical_mix * level_mix(theta)
    )
    new_salt = salt + time_step * (
        -(uvel * grad_x[:, 1] + vvel * grad_y[:, 1])
        + diffuse_rate * laplace[:, 1]
        + vertical_mix * level_mix(salt)
    )
    new_u = uvel + time_step * (
        viscosity * laplace[:, 2] + coriolis * vvel - buoyancy_scale * dens_x - drag_rate * uvel
    )
    new_v = vvel + time_step * (
        viscosity * laplace[:, 3] - coriolis * uvel - buoyancy_scale * dens_y - drag_rate * vvel
    )
    result = jnp.stack([new_theta, new_salt, new_u, new_v], axis=1)
    surface = result[:, :, 0:1] + (time_step * drive)[:, :, None]
    result = jnp.concatenate([surface, result[:, :, 1:]], axis=2)
    return result * mask[:, None]


def shards(state, forcing, cotangent, neighbour, rotation, wet, levels):
    slot_count = state.shape[0]
    group_size = lax.axis_size("tile")
    face_count = lax.axis_size("face")
    face_index = lax.axis_index("face")
    depth = jnp.arange(state.shape[2], dtype=jnp.int32)[None, :, None, None]
    mask = ((depth < levels[:, None]) & (wet[:, None, None, None] == 1)).astype(jnp.float32)
    valid = neighbour >= 0
    source = jnp.maximum(neighbour, 0)
    device_of = source // slot_count
    slot_of = source % slot_count
    source_face = device_of // group_size
    source_tile = device_of % group_size
    side = rotation % 4
    flip = rotation // 4
    lower_face = (face_index + face_count - 1) % face_count
    block = jnp.where(
        source_face == face_index,
        source_tile,
        jnp.where(source_face == lower_face, group_size, group_size + 1),
    )
    column = (block * slot_count + slot_of) * 4 + side
    total = (group_size + 2) * slot_count * 4
    selector = (
        (column[..., None] == jnp.arange(total, dtype=jnp.int32)) & valid[..., None]
    ).astype(jnp.float32)
    selector = selector.reshape(slot_count * 4, total)
    reverse = (flip == 1)[..., None, None, None]

    def gather_rims(field):
        strips = edge_strips(field)[None]
        copies = jnp.broadcast_to(strips, (group_size,) + strips.shape[1:])
        grouped = lax.all_to_all(copies, "tile", 0, 0, tiled=True)
        beside_all = with_halo(strips, (("face", 0),), 1)
        return jnp.concatenate([grouped, beside_all[0:1], beside_all[2:3]], axis=0)

    def assemble(field, candidates):
        flat = candidates.reshape(total, -1)
        chosen = jnp.dot(selector, flat, precision=lax.Precision.HIGHEST)
        chosen = chosen.reshape(slot_count, 4, field.shape[1], field.shape[2], field.shape[3])
        return jnp.where(reverse, chosen[..., ::-1], chosen)

    def fill(field):
        return assemble(field, gather_rims(field))

    def fill_back(ct_halos, field):
        cand_shape = (group_size + 2, slot_count, 4, field.shape[1], field.shape[2], field.shape[3])
        blank_cands = jnp.zeros(cand_shape, jnp.float32)
        _, pull_assemble = jax.vjp(lambda c: assemble(field, c), blank_cands)
        (ct_cands,) = pull_assemble(ct_halos)
        returned = lax.all_to_all(ct_cands[:group_size], "tile", 0, 0, tiled=True)
        back_group = jnp.sum(returned, axis=0, keepdims=True)
        back_face = with_halo(ct_cands[group_size:], (("face", 0),), 1)
        ct_strips = back_group[0] + back_face[0] + back_face[3]
        _, pull_edges = jax.vjp(edge_strips, jnp.zeros_like(field))
        (extra,) = pull_edges(ct_strips)
        return extra

    def stepper(field, halos, drive):
        return step_tiles(field, halos, mask, drive)

    first = state * mask[:, None]
    halos_first = fill(first)
    second = step_tiles(first, halos_first, mask, forcing[:, 0])
    halos_second = fill(second)
    _, pull_second = jax.vjp(stepper, second, halos_second, forcing[:, 1])
    ct_local_second, ct_halo_second, ct_drive_second = pull_second(cotangent)
    ct_second = ct_local_second + fill_back(ct_halo_second, second)
    _, pull_first = jax.vjp(stepper, first, halos_first, forcing[:, 0])
    ct_local_first, ct_halo_first, ct_drive_first = pull_first(ct_second)
    ct_first = ct_local_first + fill_back(ct_halo_first, first)
    state_gradient = ct_first * mask[:, None]
    forcing_gradient = jnp.stack([ct_drive_first, ct_drive_second], axis=1)
    return (state_gradient, forcing_gradient)


def solution(mesh):
    placed = (
        P(("face", "tile"), None, None, None, None),
        P(("face", "tile"), None, None, None, None),
        P(("face", "tile"), None, None, None, None),
        P(("face", "tile"), None),
        P(("face", "tile"), None),
        P(("face", "tile")),
        P(("face", "tile"), None, None),
    )
    return jax.shard_map(
        shards,
        mesh=mesh,
        in_specs=placed,
        out_specs=(
            P(("face", "tile"), None, None, None, None),
            P(("face", "tile"), None, None, None, None),
        ),
        check_vma=False,
    )
```

```python
import jax
import jax.numpy as jnp
from jax import lax
from jax.sharding import PartitionSpec as P

time_step = 1.0
diffuse_rate = 0.15
viscosity = 0.15
vertical_mix = 0.1
coriolis = 0.3
buoyancy_scale = 0.25
thermal_coef = 1.0
haline_coef = 0.8
drag_rate = 0.05


def with_halo(block, sides, width):
    for axis, dim in sides:
        count = lax.axis_size(axis)
        up_part = lax.slice_in_dim(block, block.shape[dim] - width, None, axis=dim)
        down_part = lax.slice_in_dim(block, 0, width, axis=dim)
        if count % 2 == 0:
            even = lax.axis_index(axis) % 2 == 0
            pairs_near = [(i, i ^ 1) for i in range(count)]
            pairs_far = [(i, (i + 1) % count if i % 2 else (i - 1) % count) for i in range(count)]
            near = lax.ppermute(jnp.where(even, up_part, down_part), axis, pairs_near)
            far = lax.ppermute(jnp.where(even, down_part, up_part), axis, pairs_far)
            low = jnp.where(even, far, near)
            high = jnp.where(even, near, far)
        else:
            forward = [(i, i + 1) for i in range(count - 1)]
            forward.append((count - 1, 0))
            backward = [(target, source) for source, target in forward]
            low = lax.ppermute(up_part, axis, forward)
            high = lax.ppermute(down_part, axis, backward)
        block = jnp.concatenate([low, block, high], axis=dim)
    return block


def edge_strips(field):
    return jnp.stack(
        [field[..., :, 0], field[..., :, -1], field[..., 0, :], field[..., -1, :]], axis=1
    )


def level_mix(values):
    above = jnp.concatenate([values[:, :1], values[:, :-1]], axis=1)
    below = jnp.concatenate([values[:, 1:], values[:, -1:]], axis=1)
    return above + below - 2.0 * values


def step_tiles(centre, halos, mask, drive):
    east = jnp.concatenate([centre[..., :, 1:], halos[:, 1][..., :, None]], axis=-1)
    west = jnp.concatenate([halos[:, 0][..., :, None], centre[..., :, :-1]], axis=-1)
    north = jnp.concatenate([centre[..., 1:, :], halos[:, 3][..., None, :]], axis=-2)
    south = jnp.concatenate([halos[:, 2][..., None, :], centre[..., :-1, :]], axis=-2)
    laplace = east + west + north + south - 4.0 * centre
    grad_x = 0.5 * (east - west)
    grad_y = 0.5 * (north - south)
    theta = centre[:, 0]
    salt = centre[:, 1]
    uvel = centre[:, 2]
    vvel = centre[:, 3]
    dens_x = -thermal_coef * grad_x[:, 0] + haline_coef * grad_x[:, 1]
    dens_y = -thermal_coef * grad_y[:, 0] + haline_coef * grad_y[:, 1]
    new_theta = theta + time_step * (
        -(uvel * grad_x[:, 0] + vvel * grad_y[:, 0])
        + diffuse_rate * laplace[:, 0]
        + vertical_mix * level_mix(theta)
    )
    new_salt = salt + time_step * (
        -(uvel * grad_x[:, 1] + vvel * grad_y[:, 1])
        + diffuse_rate * laplace[:, 1]
        + vertical_mix * level_mix(salt)
    )
    new_u = uvel + time_step * (
        viscosity * laplace[:, 2] + coriolis * vvel - buoyancy_scale * dens_x - drag_rate * uvel
    )
    new_v = vvel + time_step * (
        viscosity * laplace[:, 3] - coriolis * uvel - buoyancy_scale * dens_y - drag_rate * vvel
    )
    result = jnp.stack([new_theta, new_salt, new_u, new_v], axis=1)
    surface = result[:, :, 0:1] + (time_step * drive)[:, :, None]
    result = jnp.concatenate([surface, result[:, :, 1:]], axis=2)
    return result * mask[:, None]


def shards(state, forcing, cotangent, neighbour, rotation, wet, levels):
    slot_count = state.shape[0]
    group_size = lax.axis_size("tile")
    face_count = lax.axis_size("face")
    face_index = lax.axis_index("face")
    depth = jnp.arange(state.shape[2], dtype=jnp.int32)[None, :, None, None]
    mask = ((depth < levels[:, None]) & (wet[:, None, None, None] == 1)).astype(jnp.float32)
    valid = neighbour >= 0
    source = jnp.maximum(neighbour, 0)
    device_of = source // slot_count
    slot_of = source % slot_count
    source_face = device_of // group_size
    source_tile = device_of % group_size
    side = rotation % 4
    flip = rotation // 4
    lower_face = (face_index + face_count - 1) % face_count
    block = jnp.where(
        source_face == face_index,
        source_tile,
        jnp.where(source_face == lower_face, group_size, group_size + 1),
    )
    column = (block * slot_count + slot_of) * 4 + side
    total = (group_size + 2) * slot_count * 4
    selector = (
        (column[..., None] == jnp.arange(total, dtype=jnp.int32)) & valid[..., None]
    ).astype(jnp.float32)
    selector = selector.reshape(slot_count * 4, total)
    reverse = (flip == 1)[..., None, None, None]

    def gather_rims(field):
        strips = edge_strips(field)[None]
        copies = jnp.broadcast_to(strips, (group_size,) + strips.shape[1:])
        grouped = lax.all_to_all(copies, "tile", 0, 0, tiled=True)
        beside_all = with_halo(strips, (("face", 0),), 1)
        return jnp.concatenate([grouped, beside_all[0:1], beside_all[2:3]], axis=0)

    def assemble(field, candidates):
        flat = candidates.reshape(total, -1)
        chosen = jnp.dot(selector, flat, precision=lax.Precision.HIGHEST)
        chosen = chosen.reshape(slot_count, 4, field.shape[1], field.shape[2], field.shape[3])
        return jnp.where(reverse, chosen[..., ::-1], chosen)

    def fill(field):
        return assemble(field, gather_rims(field))

    def fill_back(ct_halos, field):
        cand_shape = (group_size + 2, slot_count, 4, field.shape[1], field.shape[2], field.shape[3])
        blank_cands = jnp.zeros(cand_shape, jnp.float32)
        _, pull_assemble = jax.vjp(lambda c: assemble(field, c), blank_cands)
        (ct_cands,) = pull_assemble(ct_halos)
        returned = lax.all_to_all(ct_cands[:group_size], "tile", 0, 0, tiled=True)
        back_group = jnp.sum(returned, axis=0, keepdims=True)
        back_face = with_halo(ct_cands[group_size:], (("face", 0),), 1)
        ct_strips = back_group[0] + back_face[0] + back_face[3]
        _, pull_edges = jax.vjp(edge_strips, jnp.zeros_like(field))
        (extra,) = pull_edges(ct_strips)
        return extra

    def stepper(field, halos, drive):
        return step_tiles(field, halos, mask, drive)

    first = state * mask[:, None]
    halos_first = fill(first)
    second = step_tiles(first, halos_first, mask, forcing[:, 0])
    halos_second = fill(second)
    _, pull_second = jax.vjp(stepper, second, halos_second, forcing[:, 1])
    ct_local_second, ct_halo_second, ct_drive_second = pull_second(cotangent)
    ct_second = ct_local_second + fill_back(ct_halo_second, second)
    _, pull_first = jax.vjp(stepper, first, halos_first, forcing[:, 0])
    ct_local_first, ct_halo_first, ct_drive_first = pull_first(ct_second)
    ct_first = ct_local_first + fill_back(ct_halo_first, first)
    state_gradient = ct_first * mask[:, None]
    forcing_gradient = jnp.stack([ct_drive_first, ct_drive_second], axis=1)
    return (state_gradient, forcing_gradient)


def solution(mesh):
    placed = (
        P(("face", "tile"), None, None, None, None),
        P(("face", "tile"), None, None, None, None),
        P(("face", "tile"), None, None, None, None),
        P(("face", "tile"), None),
        P(("face", "tile"), None),
        P(("face", "tile")),
        P(("face", "tile"), None, None),
    )
    return jax.shard_map(
        shards,
        mesh=mesh,
        in_specs=placed,
        out_specs=(
            P(("face", "tile"), None, None, None, None),
            P(("face", "tile"), None, None, None, None),
        ),
        check_vma=False,
    )
```
